32 devices in a mesh: dom: 8 (over y, x, core), dest: 4 (over z).
Axes of the slice: x: 2, y: 2, z: 4, core: 2. Of those that a mesh axis runs over, the one named last changes fastest.
Arguments:
- cost: float32 [8192], P('dom'), may hold values from 0.2 to 1.5
- turn_weight: float32 [128, 64, 512], P('dom'), may hold values from 0.0005859375 to 0.01171875
- exit_value: float32 [192, 8192], P('dest', 'dom'), may hold values from 0.05 to 1
- demand: float32 [192, 8192], P('dest', 'dom'), may hold values from 0.02 to 1
- dest_weight: float32 [192], P('dest'), may hold values from 0.3 to 3
- slot_count: int32 [128], P('dom'), may hold values from 1 to 8
- col_ref: int32 [128, 8], P('dom'), may hold values from 0 to 31, as said below
- send_blocks: int32 [8, 8, 2], replicated, may hold values from 0 to 15
Outputs:
- flows: float32 [8192], P(('dom', 'dest'))
- cost_grad: float32 [8192], P(('dom', 'dest'))
The draws below stay inside these ranges and needn't reach their ends.
Inputs may be any that keep to these rules, and one draw needn't show every extreme that they name: `col_ref`: A value below 16 names a block of the row block's own partition; a value 16 + p * 2 + c names block send_blocks[p, o, c] of partition p, o being the row block's partition.
All inputs are finite; a program needn't handle non-finite values.
Results may differ from the reference program's by a relative error of at most 0.0001.
Values sent between devices are 32-bit elements; how exact they have to be, the bound alone decides.
No kernel may reach another device: no remote copies, remote signals or barrier semaphores. Data moves between devices by JAX's collectives and lax.ppermute only.
A program may use at most 128 MiB of HBM per device.

```python
import math
import jax
import jax.numpy as jnp
from jax import lax

BLK = 64
SLOTS = 8
CAP = 2
NB_DEV = 16
DEST_DEV = 48
NBLK = 128
LINKS = 8192
DEST = 192
N_DOM = 8
N_DEST = 4


def draw_col_ref(key, part):
    kinds = jax.random.randint(jax.random.fold_in(key, 11), (NBLK, SLOTS), 0, 2)
    local_pick = jax.random.randint(jax.random.fold_in(key, 12), (NBLK, SLOTS), 0, NB_DEV)
    ghost_pick = jax.random.randint(jax.random.fold_in(key, 13), (NBLK, SLOTS), 0, N_DOM * CAP)
    refs = jnp.where(kinds == 0, local_pick, NB_DEV + ghost_pick)
    refs = refs.at[0, 0].set(NB_DEV + N_DOM * CAP - 1)
    refs = refs.at[0, 1].set(0)
    return refs.astype(jnp.int32)


def touch_ends(entries, stream_key, low, top_value):
    spot = [jax.random.randint(jax.random.fold_in(stream_key, axis), (), 0, length) for axis, length in enumerate(entries.shape)]
    longest = entries.shape.index(max(entries.shape))
    beside = spot[:longest] + [(spot[longest] + 1) % entries.shape[longest]] + spot[longest + 1:]
    return entries.at[tuple(spot)].set(low).at[tuple(beside)].set(top_value)


def steps_of(key, extent, shards, low, high):
    def one(axis_at, blocks):
        draws = jax.random.uniform(jax.random.fold_in(jax.random.fold_in(key, 6), axis_at), (blocks,), jnp.float32, low / len(shards), high / len(shards))
        return jnp.repeat(jnp.exp(draws), extent[axis_at] // blocks).reshape((-1,) + (1,) * (len(extent) - axis_at - 1))

    level = one(*shards[0])
    for cut in shards[1:]:
        level = level * one(*cut)
    return level


def setup_inputs(seed: int = 0) -> dict:
    key_of = jax.random.split(jax.random.key(seed), 9)
    cost = jnp.clip(0.2 + 1.3 * jax.random.uniform(key_of[0], (LINKS,), jnp.float32) ** steps_of(key_of[0], (LINKS,), ((0, 8),), -0.2, 0.2), 0.2, 1.5)
    turn_weight = jnp.clip(jnp.exp(math.log(0.01171875) - 2.9957322 * jax.random.uniform(key_of[1], (NBLK, BLK, SLOTS * BLK), jnp.float32) ** steps_of(key_of[1], (NBLK, BLK, SLOTS * BLK), ((0, 8),), -0.2, 0.2)), 0.0005859375, 0.01171875)
    exit_value = jnp.clip(jnp.exp(math.log(1.0) - 2.9957323 * jax.random.uniform(key_of[2], (DEST, LINKS), jnp.float32) ** steps_of(key_of[2], (DEST, LINKS), ((0, 4), (1, 8)), -0.2, 0.2)), 0.05, 1.0)
    demand = jnp.clip(jnp.exp(math.log(1.0) - 3.912023 * jax.random.uniform(key_of[3], (DEST, LINKS), jnp.float32) ** steps_of(key_of[3], (DEST, LINKS), ((0, 4), (1, 8)), -0.2, 0.2)), 0.02, 1.0)
    dest_weight = jnp.clip(jnp.exp(math.log(3.0) - 2.3025851 * jax.random.uniform(key_of[4], (DEST,), jnp.float32) ** steps_of(key_of[4], (DEST,), ((0, 4),), -0.2, 0.2)), 0.3, 3.0)
    slot_count = touch_ends(jax.random.randint(key_of[5], (NBLK,), 1, SLOTS + 1), jax.random.fold_in(key_of[5], 1), 1, SLOTS).astype(jnp.int32)
    col_ref = draw_col_ref(jax.random.fold_in(key_of[8], 71), 0)
    send_blocks = touch_ends(jax.random.randint(key_of[7], (N_DOM, N_DOM, CAP), 0, NB_DEV), jax.random.fold_in(key_of[7], 1), 0, NB_DEV - 1).astype(jnp.int32)
    return {"cost": cost, "turn_weight": turn_weight, "exit_value": exit_value, "demand": demand, "dest_weight": dest_weight, "slot_count": slot_count, "col_ref": col_ref, "send_blocks": send_blocks}


def global_columns(col_ref, send_blocks):
    owner = jnp.arange(NBLK, dtype=jnp.int32) // NB_DEV
    owner_grid = jnp.broadcast_to(owner[:, None], col_ref.shape)
    offset = jnp.maximum(col_ref - NB_DEV, 0)
    source = offset // CAP
    within = offset % CAP
    remote = source * NB_DEV + send_blocks[source, owner_grid, within]
    return jnp.where(col_ref < NB_DEV, owner_grid * NB_DEV + col_ref, remote).astype(jnp.int32)


def forward_product(field, turn_matrix, columns_global):
    rows = field.shape[0]
    picked = field.reshape(rows, NBLK, BLK)[:, columns_global, :]
    result = jnp.einsum("dnsj,nisj->dni", picked, turn_matrix, precision=lax.Precision.HIGHEST)
    return result.reshape(rows, LINKS)


def adjoint_product(field, turn_matrix, columns_global):
    rows = field.shape[0]
    terms = jnp.einsum("dni,nisj->dnsj", field.reshape(rows, NBLK, BLK), turn_matrix, precision=lax.Precision.HIGHEST)
    total = jnp.zeros((rows, NBLK, BLK), jnp.float32).at[:, columns_global, :].add(terms)
    return total.reshape(rows, LINKS)


def reference(cost, turn_weight, exit_value, demand, dest_weight, slot_count, col_ref, send_blocks):
    columns_global = global_columns(col_ref, send_blocks)
    live_slots = (jnp.arange(SLOTS, dtype=jnp.int32)[None, :] < slot_count[:, None]).astype(jnp.float32)
    turn_matrix = turn_weight.reshape(NBLK, BLK, SLOTS, BLK) * live_slots[:, None, :, None]
    link_scale = jnp.exp(-cost)

    def one_group(pieces):
        exit_part, demand_part, weight_part = pieces
        value = exit_part
        for sweep in range(2):
            value = forward_product(value * link_scale[None, :], turn_matrix, columns_global) + exit_part
        load = demand_part
        back = demand_part
        for sweep in range(2):
            ratio = load / value
            back = adjoint_product(ratio, turn_matrix, columns_global) * link_scale[None, :]
            load = value * back + demand_part
        return jnp.sum(load, axis=0), jnp.sum(weight_part[:, None] * value * back, axis=0)

    groups = (exit_value.reshape(N_DEST, DEST_DEV, LINKS), demand.reshape(N_DEST, DEST_DEV, LINKS), dest_weight.reshape(N_DEST, DEST_DEV))
    flow_parts, grad_parts = lax.map(one_group, groups)
    flows = jnp.sum(flow_parts, axis=0) / DEST
    cost_grad = -jnp.sum(grad_parts, axis=0) / DEST
    return flows, cost_grad
```

```python
import jax
import jax.numpy as jnp
from jax import lax
from jax.sharding import PartitionSpec as P

USE_PERMUTES = False
ONEHOT_SCATTER = True


def shift_pairs(count, shift):
    return [(j, (j + shift) % count) for j in range(count)]


def local(cost, turn_weight, exit_value, demand, dest_weight, slot_count, col_ref, send_blocks):
    blocks = col_ref.shape[0]
    slot_total = col_ref.shape[1]
    block_len = turn_weight.shape[1]
    columns = exit_value.shape[0]
    capacity = send_blocks.shape[2]
    partitions = lax.axis_size("dom")
    my_part = lax.axis_index("dom")
    table_blocks = blocks + partitions * capacity
    live = jnp.arange(slot_total, dtype=jnp.int32)[None, :] < slot_count[:, None]
    turn_matrix = turn_weight.reshape(blocks, block_len, slot_total, block_len) * live[
        :, None, :, None
    ].astype(jnp.float32)
    link_scale = jnp.exp(-cost)
    if USE_PERMUTES:
        ghost = jnp.maximum(col_ref - blocks, 0)
        source = ghost // capacity
        slot_of = blocks + ((my_part - source) % partitions) * capacity + ghost % capacity
        col_idx = jnp.where(col_ref < blocks, col_ref, slot_of)
        peers = (my_part + jnp.arange(partitions, dtype=jnp.int32)) % partitions
        outbound = send_blocks[my_part][peers].reshape(-1)
    else:
        col_idx = col_ref
        outbound = lax.dynamic_index_in_dim(send_blocks, my_part, 0, keepdims=False).reshape(-1)
    onehot = (
        (col_idx[:, :, None] == jnp.arange(table_blocks, dtype=jnp.int32)[None, None, :])
        & live[:, :, None]
    ).astype(jnp.float32)

    def exchange(pieces, sign):
        if not USE_PERMUTES:
            return lax.all_to_all(pieces, "dom", split_axis=1, concat_axis=1, tiled=True)
        got = [pieces[:, 0]]
        for s in range(1, partitions):
            got.append(lax.ppermute(pieces[:, s], "dom", shift_pairs(partitions, sign * s)))
        return jnp.stack(got, axis=1)

    value = exit_value
    for sweep in range(2):
        weighted = value * link_scale[None, :]
        shaped = weighted.reshape(columns, blocks, block_len)
        forward_outgoing = shaped[:, outbound, :].reshape(columns, partitions, capacity * block_len)
        received = exchange(forward_outgoing, 1)
        table = jnp.concatenate(
            [shaped, received.reshape(columns, partitions * capacity, block_len)], axis=1
        )
        picked = table[:, col_idx, :]
        result = jnp.einsum("dnsj,nisj->dni", picked, turn_matrix, precision=lax.Precision.HIGH)
        value = result.reshape(columns, blocks * block_len) + exit_value
    load = demand
    back = demand
    for sweep in range(2):
        ratio = load / value
        shaped = ratio.reshape(columns, blocks, block_len)
        terms = jnp.einsum("dni,nisj->dnsj", shaped, turn_matrix, precision=lax.Precision.HIGH)
        if ONEHOT_SCATTER:
            totals = jnp.einsum("dnsj,nsb->dbj", terms, onehot, precision=lax.Precision.HIGHEST)
        else:
            totals = (
                jnp.zeros((columns, table_blocks, block_len), jnp.float32)
                .at[:, col_idx, :]
                .add(terms)
            )
        outgoing = totals[:, blocks:, :].reshape(columns, partitions, capacity * block_len)
        returned = exchange(outgoing, -1)
        owned = (
            totals[:, :blocks, :]
            .at[:, outbound, :]
            .add(returned.reshape(columns, partitions * capacity, block_len))
        )
        back = owned.reshape(columns, blocks * block_len) * link_scale[None, :]
        load = value * back + demand
    dest_total = columns * lax.axis_size("dest")
    flow_part = jnp.sum(load, axis=0) / dest_total
    grad_part = -jnp.sum(dest_weight[:, None] * value * back, axis=0) / dest_total
    stacked = jnp.stack([flow_part, grad_part], axis=1)
    dest_n = lax.axis_size("dest")
    me = lax.axis_index("dest")
    parts = stacked.reshape(dest_n, -1, 2)
    both = lax.dynamic_index_in_dim(parts, me, 0, keepdims=False)
    for shift in range(1, dest_n):
        send = lax.dynamic_index_in_dim(parts, (me + shift) % dest_n, 0, keepdims=False)
        both = both + lax.ppermute(send, "dest", shift_pairs(dest_n, shift))
    return (both[:, 0], both[:, 1])


def solution(mesh):
    placed = (
        P("dom"),
        P("dom", None, None),
        P("dest", "dom"),
        P("dest", "dom"),
        P("dest"),
        P("dom"),
        P("dom", None),
        P(),
    )
    return jax.shard_map(
        local,
        mesh=mesh,
        in_specs=placed,
        out_specs=(P(("dom", "dest")), P(("dom", "dest"))),
        check_vma=False,
    )
```

```python
import jax
import jax.numpy as jnp
from jax import lax
from jax.experimental import pallas as pl
from jax.experimental.pallas import tpu as pltpu
from jax.sharding import PartitionSpec as P


def shift_pairs(count, shift):
    return [(j, (j + shift) % count) for j in range(count)]


def split_bf16(x):
    high = x.astype(jnp.bfloat16)
    low = (x - high.astype(jnp.float32)).astype(jnp.bfloat16)
    return high, low


def dot3(a, b):
    a_high, a_low = split_bf16(a)
    b_high, b_low = split_bf16(b)

    def one(u, v):
        return jnp.dot(u, v, preferred_element_type=jnp.float32)

    return one(a_high, b_high) + one(a_low, b_high) + one(a_high, b_low)


def forward_kernel(col_ref, table_ref, turn_ref, out_ref):
    blocks, slots = col_ref.shape
    block_len = table_ref.shape[1]
    for n in range(blocks):
        gathered = jnp.concatenate([table_ref[col_ref[n, s]] for s in range(slots)], axis=0)
        out_ref[n * block_len : (n + 1) * block_len, :] = dot3(turn_ref[n], gathered)


def adjoint_kernel(col_ref, ratio_ref, turn_ref, out_ref):
    blocks, slots = col_ref.shape
    block_len = ratio_ref.shape[0] // blocks
    out_ref[...] = jnp.zeros(out_ref.shape, out_ref.dtype)
    for n in range(blocks):
        terms = dot3(turn_ref[n], ratio_ref[n * block_len : (n + 1) * block_len, :])
        for s in range(slots):
            b = col_ref[n, s]
            out_ref[b] = out_ref[b] + terms[s * block_len : (s + 1) * block_len, :]


def local(cost, turn_weight, exit_value, demand, dest_weight, slot_count, col_ref, send_blocks):
    blocks = col_ref.shape[0]
    slot_total = col_ref.shape[1]
    block_len = turn_weight.shape[1]
    columns = exit_value.shape[0]
    capacity = send_blocks.shape[2]
    partitions = lax.axis_size("dom")
    my_part = lax.axis_index("dom")
    table_blocks = blocks + partitions * capacity
    own_len = blocks * block_len
    live = jnp.arange(slot_total, dtype=jnp.int32)[None, :] < slot_count[:, None]
    turn_matrix = turn_weight * jnp.repeat(live.astype(jnp.float32), block_len, axis=1)[:, None, :]
    turn_t = turn_matrix.transpose(0, 2, 1)
    link_scale = jnp.exp(-cost)[:, None]
    outbound = lax.dynamic_index_in_dim(send_blocks, my_part, 0, keepdims=False).reshape(-1)
    smem = pl.BlockSpec(memory_space=pltpu.SMEM)
    vmem = pl.BlockSpec(memory_space=pltpu.VMEM)
    forward = pl.pallas_call(
        forward_kernel,
        out_shape=jax.ShapeDtypeStruct((own_len, columns), jnp.float32),
        in_specs=[smem, vmem, vmem],
        out_specs=vmem,
    )
    adjoint = pl.pallas_call(
        adjoint_kernel,
        out_shape=jax.ShapeDtypeStruct((table_blocks, block_len, columns), jnp.float32),
        in_specs=[smem, vmem, vmem],
        out_specs=vmem,
    )

    def exchange(pieces):
        shaped = pieces.reshape(partitions, capacity * block_len, columns)
        got = lax.all_to_all(shaped, "dom", split_axis=0, concat_axis=0, tiled=True)
        return got.reshape(partitions * capacity, block_len, columns)

    exit_t = exit_value.T
    demand_t = demand.T
    value = exit_t
    for sweep in range(2):
        weighted = (value * link_scale).reshape(blocks, block_len, columns)
        received = exchange(weighted[outbound])
        table = jnp.concatenate([weighted, received], axis=0)
        value = forward(col_ref, table, turn_matrix) + exit_t
    load = demand_t
    back = demand_t
    for sweep in range(2):
        ratio = load / value
        totals = adjoint(col_ref, ratio, turn_t)
        returned = exchange(totals[blocks:])
        owned = totals[:blocks].at[outbound].add(returned)
        back = owned.reshape(own_len, columns) * link_scale
        load = value * back + demand_t
    dest_total = columns * lax.axis_size("dest")
    flow_part = jnp.sum(load, axis=1) / dest_total
    grad_part = -jnp.sum(dest_weight[None, :] * value * back, axis=1) / dest_total
    stacked = jnp.stack([flow_part, grad_part], axis=1)
    dest_n = lax.axis_size("dest")
    me = lax.axis_index("dest")
    parts = stacked.reshape(dest_n, -1, 2)
    both = lax.dynamic_index_in_dim(parts, me, 0, keepdims=False)
    for shift in range(1, dest_n):
        send = lax.dynamic_index_in_dim(parts, (me + shift) % dest_n, 0, keepdims=False)
        both = both + lax.ppermute(send, "dest", shift_pairs(dest_n, shift))
    return (both[:, 0], both[:, 1])


def solution(mesh):
    placed = (
        P("dom"),
        P("dom", None, None),
        P("dest", "dom"),
        P("dest", "dom"),
        P("dest"),
        P("dom"),
        P("dom", None),
        P(),
    )
    return jax.shard_map(
        local,
        mesh=mesh,
        in_specs=placed,
        out_specs=(P(("dom", "dest")), P(("dom", "dest"))),
        check_vma=False,
    )
```

```python
import jax
import jax.numpy as jnp
from jax import lax
from jax.experimental import pallas as pl
from jax.experimental.pallas import tpu as pltpu
from jax.sharding import PartitionSpec as P


def shift_pairs(count, shift):
    return [(j, (j + shift) % count) for j in range(count)]


def split_bf16(x):
    high = x.astype(jnp.bfloat16)
    low = (x - high.astype(jnp.float32)).astype(jnp.bfloat16)
    return high, low


def dot3(a, b):
    a_high, a_low = split_bf16(a)
    b_high, b_low = split_bf16(b)

    def one(u, v):
        return jnp.dot(u, v, preferred_element_type=jnp.float32)

    return one(a_high, b_high) + one(a_low, b_high) + one(a_high, b_low)


def live_factor(cnt_ref, n, s):
    return jnp.where(s < cnt_ref[n], 1.0, 0.0).astype(jnp.float32)


def add_returned(owned, out_idx_ref, returned_ref):
    block_len = owned.shape[1]
    capacity = out_idx_ref.shape[0] // returned_ref.shape[0]
    for p in range(returned_ref.shape[0]):
        got = returned_ref[p].T
        for c in range(capacity):
            b = out_idx_ref[p * capacity + c]
            owned[b] = owned[b] + got[c * block_len : (c + 1) * block_len, :]


def forward_kernel(with_send, cnt_ref, col_ref, out_idx_ref, value_ref, recv_ref, turn_ref,
                   scale_ref, exit_ref, *rest):
    if with_send:
        value_out, send_out, table = rest
    else:
        value_out, table = rest
    blocks = value_ref.shape[0]
    ghosts = out_idx_ref.shape[0]
    slots = col_ref.shape[1]
    block_len = value_ref.shape[1]
    capacity = ghosts // recv_ref.shape[0]
    table[0:blocks] = value_ref[...] * scale_ref[...]
    for p in range(recv_ref.shape[0]):
        table[blocks + p * capacity : blocks + (p + 1) * capacity] = recv_ref[p].T.reshape(
            capacity, block_len, -1
        )
    for n in range(blocks):
        pieces = [table[col_ref[n, s]] * live_factor(cnt_ref, n, s) for s in range(slots)]
        value_out[n] = dot3(turn_ref[n], jnp.concatenate(pieces, axis=0)) + exit_ref[n]
    if with_send:
        for p in range(send_out.shape[0]):
            rows = []
            for c in range(capacity):
                b = out_idx_ref[p * capacity + c]
                rows.append(value_out[b] * scale_ref[b])
            send_out[p] = jnp.concatenate(rows, axis=0).T


def adjoint_kernel(first, cnt_ref, col_ref, out_idx_ref, value_ref, demand_ref, scale_ref,
                   own_ref, returned_ref, turn_ref, own_out, ghost_out, ratio, totals):
    blocks = value_ref.shape[0]
    ghosts = out_idx_ref.shape[0]
    slots = col_ref.shape[1]
    block_len = value_ref.shape[1]
    capacity = ghosts // ghost_out.shape[0]
    if first:
        ratio[...] = demand_ref[...] / value_ref[...]
    else:
        totals[0:blocks] = own_ref[...]
        add_returned(totals, out_idx_ref, returned_ref)
        value = value_ref[...]
        load = value * (totals[0:blocks] * scale_ref[...]) + demand_ref[...]
        ratio[...] = load / value
    totals[...] = jnp.zeros(totals.shape, totals.dtype)
    for n in range(blocks):
        terms = dot3(turn_ref[n], ratio[n])
        for s in range(slots):
            b = col_ref[n, s]
            piece = terms[s * block_len : (s + 1) * block_len, :] * live_factor(cnt_ref, n, s)
            totals[b] = totals[b] + piece
    own_out[...] = totals[0:blocks]
    for p in range(ghost_out.shape[0]):
        part = totals[blocks + p * capacity : blocks + (p + 1) * capacity]
        ghost_out[p] = part.reshape(capacity * block_len, -1).T


def final_kernel(out_idx_ref, value_ref, demand_ref, scale_ref, own_ref, returned_ref, weight_ref,
                 flow_out, grad_out, owned):
    owned[...] = own_ref[...]
    add_returned(owned, out_idx_ref, returned_ref)
    value = value_ref[...]
    back = owned[...] * scale_ref[...]
    load = value * back + demand_ref[...]
    flow_out[...] = jnp.sum(load, axis=2, keepdims=True)
    grad_out[...] = jnp.sum(weight_ref[...] * value * back, axis=2, keepdims=True)


def local(cost, turn_weight, exit_value, demand, dest_weight, slot_count, col_ref, send_blocks):
    blocks = col_ref.shape[0]
    block_len = turn_weight.shape[1]
    columns = exit_value.shape[0]
    capacity = send_blocks.shape[2]
    partitions = lax.axis_size("dom")
    my_part = lax.axis_index("dom")
    ghosts = partitions * capacity
    own_len = blocks * block_len
    f32 = jnp.float32
    block_shape = (blocks, block_len, columns)
    ghost_shape = (partitions, columns, capacity * block_len)
    turn_t = turn_weight.transpose(0, 2, 1)
    scale = jnp.broadcast_to(jnp.exp(-cost).reshape(blocks, block_len, 1), block_shape)
    outbound = lax.dynamic_index_in_dim(send_blocks, my_part, 0, keepdims=False).reshape(-1)
    smem = pl.BlockSpec(memory_space=pltpu.SMEM)
    vmem = pl.BlockSpec(memory_space=pltpu.VMEM)
    scratch = pltpu.VMEM((blocks + ghosts, block_len, columns), f32)

    def forward(with_send):
        outs = [jax.ShapeDtypeStruct(block_shape, f32)]
        if with_send:
            outs.append(jax.ShapeDtypeStruct(ghost_shape, f32))
        return pl.pallas_call(
            lambda *refs: forward_kernel(with_send, *refs),
            out_shape=tuple(outs),
            in_specs=[smem, smem, smem] + [vmem] * 5,
            out_specs=tuple([vmem] * len(outs)),
            scratch_shapes=[scratch],
        )

    def adjoint(first):
        return pl.pallas_call(
            lambda *refs: adjoint_kernel(first, *refs),
            out_shape=(jax.ShapeDtypeStruct(block_shape, f32), jax.ShapeDtypeStruct(ghost_shape, f32)),
            in_specs=[smem, smem, smem] + [vmem] * 6,
            out_specs=(vmem, vmem),
            scratch_shapes=[pltpu.VMEM(block_shape, f32), scratch],
        )

    final = pl.pallas_call(
        final_kernel,
        out_shape=(
            jax.ShapeDtypeStruct((blocks, block_len, 1), f32),
            jax.ShapeDtypeStruct((blocks, block_len, 1), f32),
        ),
        in_specs=[smem] + [vmem] * 6,
        out_specs=(vmem, vmem),
        scratch_shapes=[pltpu.VMEM(block_shape, f32)],
    )

    def exchange(pieces):
        return lax.all_to_all(pieces, "dom", split_axis=0, concat_axis=0, tiled=True)

    exit_t = exit_value.T.reshape(block_shape)
    demand_t = demand.T.reshape(block_shape)
    idx = (slot_count, col_ref, outbound)
    first_send = (exit_value * jnp.exp(-cost)[None, :]).reshape(columns, blocks, block_len)[:, outbound, :]
    received = exchange(
        first_send.reshape(columns, partitions, capacity * block_len).transpose(1, 0, 2)
    )
    value, send = forward(True)(*idx, exit_t, received, turn_weight, scale, exit_t)
    received = exchange(send)
    (value,) = forward(False)(*idx, value, received, turn_weight, scale, exit_t)
    own, ghost = adjoint(True)(*idx, value, demand_t, scale, demand_t, demand_t[:1], turn_t)
    returned = exchange(ghost)
    own, ghost = adjoint(False)(*idx, value, demand_t, scale, own, returned, turn_t)
    returned = exchange(ghost)
    weight = dest_weight.reshape(1, 1, columns)
    flow_sum, grad_sum = final(outbound, value, demand_t, scale, own, returned, weight)
    dest_total = columns * lax.axis_size("dest")
    flow_part = flow_sum.reshape(own_len) / dest_total
    grad_part = -grad_sum.reshape(own_len) / dest_total
    stacked = jnp.stack([flow_part, grad_part], axis=1)
    dest_n = lax.axis_size("dest")
    me = lax.axis_index("dest")
    parts = stacked.reshape(dest_n, -1, 2)
    both = lax.dynamic_index_in_dim(parts, me, 0, keepdims=False)
    for shift in range(1, dest_n):
        send_part = lax.dynamic_index_in_dim(parts, (me + shift) % dest_n, 0, keepdims=False)
        both = both + lax.ppermute(send_part, "dest", shift_pairs(dest_n, shift))
    return (both[:, 0], both[:, 1])


def solution(mesh):
    placed = (
        P("dom"),
        P("dom", None, None),
        P("dest", "dom"),
        P("dest", "dom"),
        P("dest"),
        P("dom"),
        P("dom", None),
        P(),
    )
    return jax.shard_map(
        local,
        mesh=mesh,
        in_specs=placed,
        out_specs=(P(("dom", "dest")), P(("dom", "dest"))),
        check_vma=False,
    )
```

```python
import jax
import jax.numpy as jnp
from jax import lax
from jax.experimental import pallas as pl
from jax.experimental.pallas import tpu as pltpu
from jax.sharding import PartitionSpec as P


def shift_pairs(count, shift):
    return [(j, (j + shift) % count) for j in range(count)]


def split_bf16(x):
    high = x.astype(jnp.bfloat16)
    low = (x - high.astype(jnp.float32)).astype(jnp.bfloat16)
    return high, low


def dot3(a, b):
    a_high, a_low = split_bf16(a)
    b_high, b_low = split_bf16(b)

    def one(u, v):
        return jnp.dot(u, v, preferred_element_type=jnp.float32)

    lhs = jnp.concatenate([a_high, a_low, a_high], axis=1)
    rhs = jnp.concatenate([b_high, b_high, b_low], axis=0)
    return one(lhs, rhs)


def dest_sum(x):
    ones = jnp.ones((8, x.shape[1]), jnp.bfloat16)
    high = x.astype(jnp.bfloat16)
    rest = x - high.astype(jnp.float32)
    mid = rest.astype(jnp.bfloat16)
    low = (rest - mid.astype(jnp.float32)).astype(jnp.bfloat16)
    dims = (((1,), (1,)), ((), ()))
    total = sum(
        lax.dot_general(ones, part, dims, preferred_element_type=jnp.float32)
        for part in (high, mid, low)
    )
    return total[0:1]


def live_factor(cnt_ref, n, s):
    return jnp.where(s < cnt_ref[n], 1.0, 0.0).astype(jnp.float32)


def add_returned(owned, out_idx_ref, returned_ref):
    block_len = owned.shape[1]
    capacity = out_idx_ref.shape[0] // returned_ref.shape[0]
    for p in range(returned_ref.shape[0]):
        got = returned_ref[p][0 : owned.shape[2]].T
        for c in range(capacity):
            b = out_idx_ref[p * capacity + c]
            owned[b] = owned[b] + got[c * block_len : (c + 1) * block_len, :]


def forward_kernel(with_send, cnt_ref, col_ref, out_idx_ref, value_ref, recv_ref, turn_ref,
                   scale_ref, exit_ref, *rest):
    if with_send:
        value_out, send_out, table = rest
    else:
        value_out, table = rest
    blocks = value_ref.shape[0]
    ghosts = out_idx_ref.shape[0]
    slots = col_ref.shape[1]
    block_len = value_ref.shape[1]
    capacity = ghosts // recv_ref.shape[0]
    table[0:blocks] = value_ref[...] * scale_ref[...]
    for p in range(recv_ref.shape[0]):
        table[blocks + p * capacity : blocks + (p + 1) * capacity] = recv_ref[p].T.reshape(
            capacity, block_len, -1
        )
    for n in range(blocks):
        pieces = [table[col_ref[n, s]] * live_factor(cnt_ref, n, s) for s in range(slots)]
        value_out[n] = dot3(turn_ref[n], jnp.concatenate(pieces, axis=0)) + exit_ref[n]
    if with_send:
        for p in range(send_out.shape[0]):
            rows = []
            for c in range(capacity):
                b = out_idx_ref[p * capacity + c]
                rows.append(value_out[b] * scale_ref[b])
            send_out[p] = jnp.concatenate(rows, axis=0).T


def adjoint_kernel(first, cnt_ref, col_ref, out_idx_ref, value_ref, demand_ref, scale_ref,
                   own_ref, returned_ref, turn_ref, own_out, ghost_out, ratio, totals):
    blocks = value_ref.shape[0]
    ghosts = out_idx_ref.shape[0]
    slots = col_ref.shape[1]
    block_len = value_ref.shape[1]
    capacity = ghosts // ghost_out.shape[0]
    if first:
        ratio[...] = demand_ref[...] / value_ref[...]
    else:
        totals[0:blocks] = own_ref[...]
        add_returned(totals, out_idx_ref, returned_ref)
        value = value_ref[...]
        load = value * (totals[0:blocks] * scale_ref[...]) + demand_ref[...]
        ratio[...] = load / value
    totals[...] = jnp.zeros(totals.shape, totals.dtype)
    for n in range(blocks):
        terms = dot3(turn_ref[n], ratio[n])
        for s in range(slots):
            b = col_ref[n, s]
            piece = terms[s * block_len : (s + 1) * block_len, :] * live_factor(cnt_ref, n, s)
            totals[b] = totals[b] + piece
    own_out[...] = totals[0:blocks]
    for p in range(ghost_out.shape[0]):
        part = totals[blocks + p * capacity : blocks + (p + 1) * capacity]
        ghost_out[p] = part.reshape(capacity * block_len, -1).T


def last_kernel(cnt_ref, col_ref, out_idx_ref, value_ref, demand_ref, scale_ref, own_ref,
                returned_ref, turn_ref, weight_ref, sums_out, ratio, totals):
    blocks = value_ref.shape[0]
    ghosts = out_idx_ref.shape[0]
    slots = col_ref.shape[1]
    block_len = value_ref.shape[1]
    columns = value_ref.shape[2]
    capacity = ghosts // returned_ref.shape[0]
    totals[0:blocks] = own_ref[...]
    add_returned(totals, out_idx_ref, returned_ref)
    value = value_ref[...]
    load = value * (totals[0:blocks] * scale_ref[...]) + demand_ref[...]
    ratio[...] = load / value
    totals[...] = jnp.zeros(totals.shape, totals.dtype)
    for n in range(blocks):
        terms = dot3(turn_ref[n], ratio[n])
        for s in range(slots):
            b = col_ref[n, s]
            piece = terms[s * block_len : (s + 1) * block_len, :] * live_factor(cnt_ref, n, s)
            totals[b] = totals[b] + piece
    weight = weight_ref[...]
    for b in range(blocks):
        product = value_ref[b] * scale_ref[b] * totals[b]
        sums_out[0, b : b + 1, :] = dest_sum(product + demand_ref[b])
        sums_out[1, b : b + 1, :] = dest_sum(weight * product)
    for p in range(returned_ref.shape[0]):
        weighted = returned_ref[p][columns : 2 * columns].T
        for c in range(capacity):
            k = p * capacity + c
            product = weighted[c * block_len : (c + 1) * block_len, :] * totals[blocks + k]
            sums_out[0, blocks + k : blocks + k + 1, :] = dest_sum(product)
            sums_out[1, blocks + k : blocks + k + 1, :] = dest_sum(weight * product)


def final_kernel(out_idx_ref, value_ref, demand_ref, scale_ref, own_ref, returned_ref, weight_ref,
                 flow_out, grad_out, owned):
    owned[...] = own_ref[...]
    add_returned(owned, out_idx_ref, returned_ref)
    value = value_ref[...]
    back = owned[...] * scale_ref[...]
    load = value * back + demand_ref[...]
    flow_out[...] = jnp.sum(load, axis=2, keepdims=True)
    grad_out[...] = jnp.sum(weight_ref[...] * value * back, axis=2, keepdims=True)


def local(cost, turn_weight, exit_value, demand, dest_weight, slot_count, col_ref, send_blocks):
    blocks = col_ref.shape[0]
    block_len = turn_weight.shape[1]
    columns = exit_value.shape[0]
    capacity = send_blocks.shape[2]
    partitions = lax.axis_size("dom")
    my_part = lax.axis_index("dom")
    ghosts = partitions * capacity
    own_len = blocks * block_len
    f32 = jnp.float32
    block_shape = (blocks, block_len, columns)
    ghost_shape = (partitions, columns, capacity * block_len)
    turn_t = turn_weight.transpose(0, 2, 1)
    scale = jnp.broadcast_to(jnp.exp(-cost).reshape(blocks, block_len, 1), block_shape)
    outbound = lax.dynamic_index_in_dim(send_blocks, my_part, 0, keepdims=False).reshape(-1)
    smem = pl.BlockSpec(memory_space=pltpu.SMEM)
    vmem = pl.BlockSpec(memory_space=pltpu.VMEM)
    scratch = pltpu.VMEM((blocks + ghosts, block_len, columns), f32)

    def forward(with_send):
        outs = [jax.ShapeDtypeStruct(block_shape, f32)]
        if with_send:
            outs.append(jax.ShapeDtypeStruct(ghost_shape, f32))
        return pl.pallas_call(
            lambda *refs: forward_kernel(with_send, *refs),
            out_shape=tuple(outs),
            in_specs=[smem, smem, smem] + [vmem] * 5,
            out_specs=tuple([vmem] * len(outs)),
            scratch_shapes=[scratch],
        )

    def adjoint(first):
        return pl.pallas_call(
            lambda *refs: adjoint_kernel(first, *refs),
            out_shape=(jax.ShapeDtypeStruct(block_shape, f32), jax.ShapeDtypeStruct(ghost_shape, f32)),
            in_specs=[smem, smem, smem] + [vmem] * 6,
            out_specs=(vmem, vmem),
            scratch_shapes=[pltpu.VMEM(block_shape, f32), scratch],
        )

    final = pl.pallas_call(
        final_kernel,
        out_shape=(
            jax.ShapeDtypeStruct((blocks, block_len, 1), f32),
            jax.ShapeDtypeStruct((blocks, block_len, 1), f32),
        ),
        in_specs=[smem] + [vmem] * 6,
        out_specs=(vmem, vmem),
        scratch_shapes=[pltpu.VMEM(block_shape, f32)],
    )

    def exchange(pieces):
        return lax.all_to_all(pieces, "dom", split_axis=0, concat_axis=0, tiled=True)

    exit_t = exit_value.T.reshape(block_shape)
    demand_t = demand.T.reshape(block_shape)
    idx = (slot_count, col_ref, outbound)
    first_send = (exit_value * jnp.exp(-cost)[None, :]).reshape(columns, blocks, block_len)[:, outbound, :]
    received = exchange(
        first_send.reshape(columns, partitions, capacity * block_len).transpose(1, 0, 2)
    )
    value, send = forward(True)(*idx, exit_t, received, turn_weight, scale, exit_t)
    received = exchange(send)
    value, send = forward(True)(*idx, value, received, turn_weight, scale, exit_t)
    own, ghost = adjoint(True)(*idx, value, demand_t, scale, demand_t, demand_t[:1], turn_t)
    returned = exchange(jnp.concatenate([ghost, send], axis=1))
    weight = dest_weight.reshape(1, columns)
    last = pl.pallas_call(
        last_kernel,
        out_shape=jax.ShapeDtypeStruct((2, blocks + ghosts, block_len), f32),
        in_specs=[smem, smem, smem] + [vmem] * 7,
        out_specs=vmem,
        scratch_shapes=[pltpu.VMEM(block_shape, f32), scratch],
    )
    sums = last(*idx, value, demand_t, scale, own, returned, turn_t, weight)
    dest_n = lax.axis_size("dest")
    ghost_part = jnp.arange(ghosts, dtype=jnp.int32) // capacity
    ghost_block = send_blocks[ghost_part, my_part, jnp.arange(ghosts, dtype=jnp.int32) % capacity]
    routed = jnp.zeros((partitions, blocks, 2, block_len), f32)
    routed = lax.dynamic_update_index_in_dim(routed, sums[:, :blocks].transpose(1, 0, 2), my_part, 0)
    routed = routed.at[ghost_part, ghost_block].add(sums[:, blocks:].transpose(1, 0, 2))
    routed = routed.reshape(partitions * dest_n, blocks // dest_n, 2, block_len)
    got = lax.all_to_all(routed, ("dom", "dest"), split_axis=0, concat_axis=0, tiled=True)
    total = jnp.sum(got, axis=0) / (columns * dest_n)
    return (total[:, 0].reshape(-1), -total[:, 1].reshape(-1))


def solution(mesh):
    placed = (
        P("dom"),
        P("dom", None, None),
        P("dest", "dom"),
        P("dest", "dom"),
        P("dest"),
        P("dom"),
        P("dom", None),
        P(),
    )
    return jax.shard_map(
        local,
        mesh=mesh,
        in_specs=placed,
        out_specs=(P(("dom", "dest")), P(("dom", "dest"))),
        check_vma=False,
    )
```

```python
import jax
import jax.numpy as jnp
from jax import lax
from jax.experimental import pallas as pl
from jax.experimental.pallas import tpu as pltpu
from jax.sharding import PartitionSpec as P


def shift_pairs(count, shift):
    return [(j, (j + shift) % count) for j in range(count)]


def split_bf16(x):
    high = x.astype(jnp.bfloat16)
    low = (x - high.astype(jnp.float32)).astype(jnp.bfloat16)
    return high, low


def dot3(a, b):
    a_high, a_low = split_bf16(a)
    b_high, b_low = split_bf16(b)

    def one(u, v):
        return jnp.dot(u, v, preferred_element_type=jnp.float32)

    lhs = jnp.concatenate([a_high, a_low, a_high], axis=1)
    rhs = jnp.concatenate([b_high, b_high, b_low], axis=0)
    return one(lhs, rhs)


def dest_sum(x):
    ones = jnp.ones((8, x.shape[1]), jnp.bfloat16)
    high = x.astype(jnp.bfloat16)
    rest = x - high.astype(jnp.float32)
    mid = rest.astype(jnp.bfloat16)
    low = (rest - mid.astype(jnp.float32)).astype(jnp.bfloat16)
    dims = (((1,), (1,)), ((), ()))
    total = sum(
        lax.dot_general(ones, part, dims, preferred_element_type=jnp.float32)
        for part in (high, mid, low)
    )
    return total[0:1]


def live_factor(cnt_ref, n, s):
    return jnp.where(s < cnt_ref[n], 1.0, 0.0).astype(jnp.float32)


def add_returned(owned, out_idx_ref, returned_ref):
    block_len = owned.shape[1]
    capacity = out_idx_ref.shape[0] // returned_ref.shape[0]
    for p in range(returned_ref.shape[0]):
        got = returned_ref[p][0 : owned.shape[2]].T
        for c in range(capacity):
            b = out_idx_ref[p * capacity + c]
            owned[b] = owned[b] + got[c * block_len : (c + 1) * block_len, :]


def forward_kernel(with_send, cnt_ref, col_ref, out_idx_ref, value_ref, recv_ref, turn_ref,
                   scale_ref, exit_ref, *rest):
    if with_send:
        value_out, send_out, table = rest
    else:
        value_out, table = rest
    blocks = value_ref.shape[0]
    ghosts = out_idx_ref.shape[0]
    slots = col_ref.shape[1]
    block_len = value_ref.shape[1]
    capacity = ghosts // recv_ref.shape[0]
    table[0:blocks] = value_ref[...] * scale_ref[...]
    for p in range(recv_ref.shape[0]):
        table[blocks + p * capacity : blocks + (p + 1) * capacity] = recv_ref[p].T.reshape(
            capacity, block_len, -1
        )
    for n in range(blocks):
        pieces = [table[col_ref[n, s]] * live_factor(cnt_ref, n, s) for s in range(slots)]
        value_out[n] = dot3(turn_ref[n], jnp.concatenate(pieces, axis=0)) + exit_ref[n]
    if with_send:
        for p in range(send_out.shape[0]):
            rows = []
            for c in range(capacity):
                b = out_idx_ref[p * capacity + c]
                rows.append(value_out[b] * scale_ref[b])
            send_out[p] = jnp.concatenate(rows, axis=0).T


def adjoint_kernel(first, cnt_ref, col_ref, out_idx_ref, value_ref, demand_ref, scale_ref,
                   own_ref, returned_ref, turn_ref, extra_ref, own_out, ghost_out, ratio, totals):
    blocks = value_ref.shape[0]
    ghosts = out_idx_ref.shape[0]
    slots = col_ref.shape[1]
    block_len = value_ref.shape[1]
    capacity = ghosts // ghost_out.shape[0]
    if first:
        ratio[...] = demand_ref[...] / value_ref[...]
    else:
        totals[0:blocks] = own_ref[...]
        add_returned(totals, out_idx_ref, returned_ref)
        value = value_ref[...]
        load = value * (totals[0:blocks] * scale_ref[...]) + demand_ref[...]
        ratio[...] = load / value
    totals[...] = jnp.zeros(totals.shape, totals.dtype)
    for n in range(blocks):
        terms = dot3(turn_ref[n], ratio[n])
        for s in range(slots):
            b = col_ref[n, s]
            piece = terms[s * block_len : (s + 1) * block_len, :] * live_factor(cnt_ref, n, s)
            totals[b] = totals[b] + piece
    own_out[...] = totals[0:blocks]
    for p in range(ghost_out.shape[0]):
        part = totals[blocks + p * capacity : blocks + (p + 1) * capacity]
        ghost_out[p, 0 : value_ref.shape[2]] = part.reshape(capacity * block_len, -1).T
        ghost_out[p, value_ref.shape[2] :] = extra_ref[p]


def last_kernel(cnt_ref, col_ref, out_idx_ref, place_ref, value_ref, demand_ref, scale_ref, own_ref,
                returned_ref, turn_ref, weight_ref, routed_out, ratio, totals):
    blocks = value_ref.shape[0]
    ghosts = out_idx_ref.shape[0]
    slots = col_ref.shape[1]
    block_len = value_ref.shape[1]
    columns = value_ref.shape[2]
    capacity = ghosts // returned_ref.shape[0]
    totals[0:blocks] = own_ref[...]
    add_returned(totals, out_idx_ref, returned_ref)
    value = value_ref[...]
    load = value * (totals[0:blocks] * scale_ref[...]) + demand_ref[...]
    ratio[...] = load / value
    totals[...] = jnp.zeros(totals.shape, totals.dtype)
    for n in range(blocks):
        terms = dot3(turn_ref[n], ratio[n])
        for s in range(slots):
            b = col_ref[n, s]
            piece = terms[s * block_len : (s + 1) * block_len, :] * live_factor(cnt_ref, n, s)
            totals[b] = totals[b] + piece
    weight = weight_ref[...]
    routed_out[...] = jnp.zeros(routed_out.shape, routed_out.dtype)
    me = place_ref[0]
    for b in range(blocks):
        product = value_ref[b] * scale_ref[b] * totals[b]
        routed_out[me, b, 0:1, :] = dest_sum(product + demand_ref[b])
        routed_out[me, b, 1:2, :] = dest_sum(weight * product)
    for p in range(returned_ref.shape[0]):
        weighted = returned_ref[p][columns : 2 * columns].T
        for c in range(capacity):
            k = p * capacity + c
            blk = place_ref[1 + k]
            product = weighted[c * block_len : (c + 1) * block_len, :] * totals[blocks + k]
            routed_out[p, blk, 0:1, :] = routed_out[p, blk, 0:1, :] + dest_sum(product)
            routed_out[p, blk, 1:2, :] = routed_out[p, blk, 1:2, :] + dest_sum(weight * product)


def final_kernel(out_idx_ref, value_ref, demand_ref, scale_ref, own_ref, returned_ref, weight_ref,
                 flow_out, grad_out, owned):
    owned[...] = own_ref[...]
    add_returned(owned, out_idx_ref, returned_ref)
    value = value_ref[...]
    back = owned[...] * scale_ref[...]
    load = value * back + demand_ref[...]
    flow_out[...] = jnp.sum(load, axis=2, keepdims=True)
    grad_out[...] = jnp.sum(weight_ref[...] * value * back, axis=2, keepdims=True)


def local(cost, turn_weight, exit_value, demand, dest_weight, slot_count, col_ref, send_blocks):
    blocks = col_ref.shape[0]
    block_len = turn_weight.shape[1]
    columns = exit_value.shape[0]
    capacity = send_blocks.shape[2]
    partitions = lax.axis_size("dom")
    my_part = lax.axis_index("dom")
    ghosts = partitions * capacity
    own_len = blocks * block_len
    f32 = jnp.float32
    block_shape = (blocks, block_len, columns)
    ghost_shape = (partitions, columns, capacity * block_len)
    turn_t = turn_weight.transpose(0, 2, 1)
    scale = jnp.broadcast_to(jnp.exp(-cost).reshape(blocks, block_len, 1), block_shape)
    outbound = lax.dynamic_index_in_dim(send_blocks, my_part, 0, keepdims=False).reshape(-1)
    smem = pl.BlockSpec(memory_space=pltpu.SMEM)
    vmem = pl.BlockSpec(memory_space=pltpu.VMEM)
    scratch = pltpu.VMEM((blocks + ghosts, block_len, columns), f32)

    def forward(with_send):
        outs = [jax.ShapeDtypeStruct(block_shape, f32)]
        if with_send:
            outs.append(jax.ShapeDtypeStruct(ghost_shape, f32))
        return pl.pallas_call(
            lambda *refs: forward_kernel(with_send, *refs),
            out_shape=tuple(outs),
            in_specs=[smem, smem, smem] + [vmem] * 5,
            out_specs=tuple([vmem] * len(outs)),
            scratch_shapes=[scratch],
        )

    def adjoint(first):
        doubled = (partitions, 2 * columns, capacity * block_len)
        return pl.pallas_call(
            lambda *refs: adjoint_kernel(first, *refs),
            out_shape=(jax.ShapeDtypeStruct(block_shape, f32), jax.ShapeDtypeStruct(doubled, f32)),
            in_specs=[smem, smem, smem] + [vmem] * 7,
            out_specs=(vmem, vmem),
            scratch_shapes=[pltpu.VMEM(block_shape, f32), scratch],
        )

    final = pl.pallas_call(
        final_kernel,
        out_shape=(
            jax.ShapeDtypeStruct((blocks, block_len, 1), f32),
            jax.ShapeDtypeStruct((blocks, block_len, 1), f32),
        ),
        in_specs=[smem] + [vmem] * 6,
        out_specs=(vmem, vmem),
        scratch_shapes=[pltpu.VMEM(block_shape, f32)],
    )

    def exchange(pieces):
        return lax.all_to_all(pieces, "dom", split_axis=0, concat_axis=0, tiled=True)

    exit_t = exit_value.T.reshape(block_shape)
    demand_t = demand.T.reshape(block_shape)
    idx = (slot_count, col_ref, outbound)
    first_send = (exit_value * jnp.exp(-cost)[None, :]).reshape(columns, blocks, block_len)[:, outbound, :]
    received = exchange(
        first_send.reshape(columns, partitions, capacity * block_len).transpose(1, 0, 2)
    )
    value, send = forward(True)(*idx, exit_t, received, turn_weight, scale, exit_t)
    received = exchange(send)
    value, send = forward(True)(*idx, value, received, turn_weight, scale, exit_t)
    own, ghost = adjoint(True)(*idx, value, demand_t, scale, demand_t, demand_t[:1], turn_t, send)
    returned = exchange(ghost)
    weight = dest_weight.reshape(1, columns)
    ghost_part = jnp.arange(ghosts, dtype=jnp.int32) // capacity
    ghost_block = send_blocks[ghost_part, my_part, jnp.arange(ghosts, dtype=jnp.int32) % capacity]
    place = jnp.concatenate([my_part.astype(jnp.int32).reshape(1), ghost_block.astype(jnp.int32)])
    last = pl.pallas_call(
        last_kernel,
        out_shape=jax.ShapeDtypeStruct((partitions, blocks, 2, block_len), f32),
        in_specs=[smem, smem, smem, smem] + [vmem] * 7,
        out_specs=vmem,
        scratch_shapes=[pltpu.VMEM(block_shape, f32), scratch],
    )
    routed = last(*idx, place, value, demand_t, scale, own, returned, turn_t, weight)
    dest_n = lax.axis_size("dest")
    routed = routed.reshape(partitions * dest_n, blocks // dest_n, 2, block_len)
    got = lax.all_to_all(routed, ("dom", "dest"), split_axis=0, concat_axis=0, tiled=True)
    total = jnp.sum(got, axis=0) / (columns * dest_n)
    return (total[:, 0].reshape(-1), -total[:, 1].reshape(-1))


def solution(mesh):
    placed = (
        P("dom"),
        P("dom", None, None),
        P("dest", "dom"),
        P("dest", "dom"),
        P("dest"),
        P("dom"),
        P("dom", None),
        P(),
    )
    return jax.shard_map(
        local,
        mesh=mesh,
        in_specs=placed,
        out_specs=(P(("dom", "dest")), P(("dom", "dest"))),
        check_vma=False,
    )
```

```python
import jax
import jax.numpy as jnp
from jax import lax
from jax.experimental import pallas as pl
from jax.experimental.pallas import tpu as pltpu
from jax.sharding import PartitionSpec as P


def shift_pairs(count, shift):
    return [(j, (j + shift) % count) for j in range(count)]


def split_bf16(x):
    high = x.astype(jnp.bfloat16)
    low = (x - high.astype(jnp.float32)).astype(jnp.bfloat16)
    return high, low


def dot3(a, b):
    a_high, a_low = split_bf16(a)
    b_high, b_low = split_bf16(b)

    def one(u, v):
        return jnp.dot(u, v, preferred_element_type=jnp.float32)

    lhs = jnp.concatenate([a_high, a_low, a_high], axis=1)
    rhs = jnp.concatenate([b_high, b_high, b_low], axis=0)
    return one(lhs, rhs)


def dest_sum(x):
    ones = jnp.ones((8, x.shape[1]), jnp.bfloat16)
    high, low = split_bf16(x)
    dims = (((1,), (1,)), ((), ()))
    parts = jnp.concatenate([high, low], axis=0)
    total = lax.dot_general(ones, parts, dims, preferred_element_type=jnp.float32)
    total = total[:, 0 : x.shape[0]] + total[:, x.shape[0] :]
    return total[0:1]


def live_factor(cnt_ref, n, s):
    return jnp.where(s < cnt_ref[n], 1.0, 0.0).astype(jnp.float32)


def add_returned(owned, out_idx_ref, returned_ref):
    block_len = owned.shape[1]
    capacity = out_idx_ref.shape[0] // returned_ref.shape[0]
    for p in range(returned_ref.shape[0]):
        got = returned_ref[p][0 : owned.shape[2]].T
        for c in range(capacity):
            b = out_idx_ref[p * capacity + c]
            owned[b] = owned[b] + got[c * block_len : (c + 1) * block_len, :]


def forward_kernel(with_send, cnt_ref, col_ref, out_idx_ref, value_ref, recv_ref, turn_ref,
                   scale_ref, exit_ref, *rest):
    if with_send:
        value_out, send_out, table = rest
    else:
        value_out, table = rest
    blocks = value_ref.shape[0]
    ghosts = out_idx_ref.shape[0]
    slots = col_ref.shape[1]
    block_len = value_ref.shape[1]
    capacity = ghosts // recv_ref.shape[0]
    table[0:blocks] = value_ref[...] * scale_ref[...]
    for p in range(recv_ref.shape[0]):
        table[blocks + p * capacity : blocks + (p + 1) * capacity] = recv_ref[p].T.reshape(
            capacity, block_len, -1
        )
    for n in range(blocks):
        pieces = [table[col_ref[n, s]] * live_factor(cnt_ref, n, s) for s in range(slots)]
        value_out[n] = dot3(turn_ref[n], jnp.concatenate(pieces, axis=0)) + exit_ref[n]
    if with_send:
        for p in range(send_out.shape[0]):
            rows = []
            for c in range(capacity):
                b = out_idx_ref[p * capacity + c]
                rows.append(value_out[b] * scale_ref[b])
            send_out[p] = jnp.concatenate(rows, axis=0).T


def adjoint_kernel(first, cnt_ref, col_ref, out_idx_ref, value_ref, demand_ref, scale_ref,
                   own_ref, returned_ref, turn_ref, extra_ref, own_out, ghost_out, ratio, totals):
    blocks = value_ref.shape[0]
    ghosts = out_idx_ref.shape[0]
    slots = col_ref.shape[1]
    block_len = value_ref.shape[1]
    capacity = ghosts // ghost_out.shape[0]
    if first:
        ratio[...] = demand_ref[...] / value_ref[...]
    else:
        totals[0:blocks] = own_ref[...]
        add_returned(totals, out_idx_ref, returned_ref)
        value = value_ref[...]
        load = value * (totals[0:blocks] * scale_ref[...]) + demand_ref[...]
        ratio[...] = load / value
    totals[...] = jnp.zeros(totals.shape, totals.dtype)
    for n in range(blocks):
        terms = dot3(turn_ref[n], ratio[n])
        for s in range(slots):
            b = col_ref[n, s]
            piece = terms[s * block_len : (s + 1) * block_len, :] * live_factor(cnt_ref, n, s)
            totals[b] = totals[b] + piece
    own_out[...] = totals[0:blocks]
    for p in range(ghost_out.shape[0]):
        part = totals[blocks + p * capacity : blocks + (p + 1) * capacity]
        ghost_out[p, 0 : value_ref.shape[2]] = part.reshape(capacity * block_len, -1).T
        ghost_out[p, value_ref.shape[2] :] = extra_ref[p]


def last_kernel(cnt_ref, col_ref, out_idx_ref, place_ref, value_ref, demand_ref, scale_ref, own_ref,
                returned_ref, turn_ref, weight_ref, routed_out, ratio, totals):
    blocks = value_ref.shape[0]
    ghosts = out_idx_ref.shape[0]
    slots = col_ref.shape[1]
    block_len = value_ref.shape[1]
    columns = value_ref.shape[2]
    capacity = ghosts // returned_ref.shape[0]
    totals[0:blocks] = own_ref[...]
    add_returned(totals, out_idx_ref, returned_ref)
    value = value_ref[...]
    load = value * (totals[0:blocks] * scale_ref[...]) + demand_ref[...]
    ratio[...] = load / value
    totals[...] = jnp.zeros(totals.shape, totals.dtype)
    for n in range(blocks):
        terms = dot3(turn_ref[n], ratio[n])
        for s in range(slots):
            b = col_ref[n, s]
            piece = terms[s * block_len : (s + 1) * block_len, :] * live_factor(cnt_ref, n, s)
            totals[b] = totals[b] + piece
    weight = weight_ref[...]
    routed_out[...] = jnp.zeros(routed_out.shape, routed_out.dtype)
    me = place_ref[0]
    for b in range(blocks):
        product = value_ref[b] * scale_ref[b] * totals[b]
        routed_out[me, b, 0:1, :] = dest_sum(product + demand_ref[b])
        routed_out[me, b, 1:2, :] = dest_sum(weight * product)
    for p in range(returned_ref.shape[0]):
        weighted = returned_ref[p][columns : 2 * columns].T
        for c in range(capacity):
            k = p * capacity + c
            blk = place_ref[1 + k]
            product = weighted[c * block_len : (c + 1) * block_len, :] * totals[blocks + k]
            routed_out[p, blk, 0:1, :] = routed_out[p, blk, 0:1, :] + dest_sum(product)
            routed_out[p, blk, 1:2, :] = routed_out[p, blk, 1:2, :] + dest_sum(weight * product)


def final_kernel(out_idx_ref, value_ref, demand_ref, scale_ref, own_ref, returned_ref, weight_ref,
                 flow_out, grad_out, owned):
    owned[...] = own_ref[...]
    add_returned(owned, out_idx_ref, returned_ref)
    value = value_ref[...]
    back = owned[...] * scale_ref[...]
    load = value * back + demand_ref[...]
    flow_out[...] = jnp.sum(load, axis=2, keepdims=True)
    grad_out[...] = jnp.sum(weight_ref[...] * value * back, axis=2, keepdims=True)


def local(cost, turn_weight, exit_value, demand, dest_weight, slot_count, col_ref, send_blocks):
    blocks = col_ref.shape[0]
    block_len = turn_weight.shape[1]
    columns = exit_value.shape[0]
    capacity = send_blocks.shape[2]
    partitions = lax.axis_size("dom")
    my_part = lax.axis_index("dom")
    ghosts = partitions * capacity
    own_len = blocks * block_len
    f32 = jnp.float32
    block_shape = (blocks, block_len, columns)
    ghost_shape = (partitions, columns, capacity * block_len)
    turn_t = turn_weight.transpose(0, 2, 1)
    scale = jnp.broadcast_to(jnp.exp(-cost).reshape(blocks, block_len, 1), block_shape)
    outbound = lax.dynamic_index_in_dim(send_blocks, my_part, 0, keepdims=False).reshape(-1)
    smem = pl.BlockSpec(memory_space=pltpu.SMEM)
    vmem = pl.BlockSpec(memory_space=pltpu.VMEM)
    scratch = pltpu.VMEM((blocks + ghosts, block_len, columns), f32)

    def forward(with_send):
        outs = [jax.ShapeDtypeStruct(block_shape, f32)]
        if with_send:
            outs.append(jax.ShapeDtypeStruct(ghost_shape, f32))
        return pl.pallas_call(
            lambda *refs: forward_kernel(with_send, *refs),
            out_shape=tuple(outs),
            in_specs=[smem, smem, smem] + [vmem] * 5,
            out_specs=tuple([vmem] * len(outs)),
            scratch_shapes=[scratch],
        )

    def adjoint(first):
        doubled = (partitions, 2 * columns, capacity * block_len)
        return pl.pallas_call(
            lambda *refs: adjoint_kernel(first, *refs),
            out_shape=(jax.ShapeDtypeStruct(block_shape, f32), jax.ShapeDtypeStruct(doubled, f32)),
            in_specs=[smem, smem, smem] + [vmem] * 7,
            out_specs=(vmem, vmem),
            scratch_shapes=[pltpu.VMEM(block_shape, f32), scratch],
        )

    final = pl.pallas_call(
        final_kernel,
        out_shape=(
            jax.ShapeDtypeStruct((blocks, block_len, 1), f32),
            jax.ShapeDtypeStruct((blocks, block_len, 1), f32),
        ),
        in_specs=[smem] + [vmem] * 6,
        out_specs=(vmem, vmem),
        scratch_shapes=[pltpu.VMEM(block_shape, f32)],
    )

    def exchange(pieces):
        return lax.all_to_all(pieces, "dom", split_axis=0, concat_axis=0, tiled=True)

    exit_t = exit_value.T.reshape(block_shape)
    demand_t = demand.T.reshape(block_shape)
    idx = (slot_count, col_ref, outbound)
    first_send = (exit_value * jnp.exp(-cost)[None, :]).reshape(columns, blocks, block_len)[:, outbound, :]
    received = exchange(
        first_send.reshape(columns, partitions, capacity * block_len).transpose(1, 0, 2)
    )
    value, send = forward(True)(*idx, exit_t, received, turn_weight, scale, exit_t)
    received = exchange(send)
    value, send = forward(True)(*idx, value, received, turn_weight, scale, exit_t)
    own, ghost = adjoint(True)(*idx, value, demand_t, scale, demand_t, demand_t[:1], turn_t, send)
    returned = exchange(ghost)
    weight = dest_weight.reshape(1, columns)
    ghost_part = jnp.arange(ghosts, dtype=jnp.int32) // capacity
    ghost_block = send_blocks[ghost_part, my_part, jnp.arange(ghosts, dtype=jnp.int32) % capacity]
    place = jnp.concatenate([my_part.astype(jnp.int32).reshape(1), ghost_block.astype(jnp.int32)])
    last = pl.pallas_call(
        last_kernel,
        out_shape=jax.ShapeDtypeStruct((partitions, blocks, 2, block_len), f32),
        in_specs=[smem, smem, smem, smem] + [vmem] * 7,
        out_specs=vmem,
        scratch_shapes=[pltpu.VMEM(block_shape, f32), scratch],
    )
    routed = last(*idx, place, value, demand_t, scale, own, returned, turn_t, weight)
    dest_n = lax.axis_size("dest")
    routed = routed.reshape(partitions * dest_n, blocks // dest_n, 2, block_len)
    got = lax.all_to_all(routed, ("dom", "dest"), split_axis=0, concat_axis=0, tiled=True)
    total = jnp.sum(got, axis=0) / (columns * dest_n)
    return (total[:, 0].reshape(-1), -total[:, 1].reshape(-1))


def solution(mesh):
    placed = (
        P("dom"),
        P("dom", None, None),
        P("dest", "dom"),
        P("dest", "dom"),
        P("dest"),
        P("dom"),
        P("dom", None),
        P(),
    )
    return jax.shard_map(
        local,
        mesh=mesh,
        in_specs=placed,
        out_specs=(P(("dom", "dest")), P(("dom", "dest"))),
        check_vma=False,
    )
```

```python
import jax
import jax.numpy as jnp
from jax import lax
from jax.experimental import pallas as pl
from jax.experimental.pallas import tpu as pltpu
from jax.sharding import PartitionSpec as P


def shift_pairs(count, shift):
    return [(j, (j + shift) % count) for j in range(count)]


def split_bf16(x):
    high = x.astype(jnp.bfloat16)
    low = (x - high.astype(jnp.float32)).astype(jnp.bfloat16)
    return high, low


def dot3(a, b):
    a_high, a_low = split_bf16(a)
    b_high, b_low = split_bf16(b)

    def one(u, v):
        return jnp.dot(u, v, preferred_element_type=jnp.float32)

    lhs = jnp.concatenate([a_high, a_low, a_high], axis=1)
    rhs = jnp.concatenate([b_high, b_high, b_low], axis=0)
    return one(lhs, rhs)


def dest_sum(x):
    ones = jnp.ones((8, x.shape[1]), jnp.bfloat16)
    high, low = split_bf16(x)
    dims = (((1,), (1,)), ((), ()))
    parts = jnp.concatenate([high, low], axis=0)
    total = lax.dot_general(ones, parts, dims, preferred_element_type=jnp.float32)
    total = total[:, 0 : x.shape[0]] + total[:, x.shape[0] :]
    return total[0:1]


def live_factor(cnt_ref, n, s):
    return jnp.where(s < cnt_ref[n], 1.0, 0.0).astype(jnp.float32)


def add_returned(owned, out_idx_ref, returned_ref):
    block_len = owned.shape[1]
    capacity = out_idx_ref.shape[0] // returned_ref.shape[0]
    for p in range(returned_ref.shape[0]):
        got = returned_ref[p][0 : owned.shape[2]].T
        for c in range(capacity):
            b = out_idx_ref[p * capacity + c]
            owned[b] = owned[b] + got[c * block_len : (c + 1) * block_len, :]


def forward_kernel(with_send, cnt_ref, col_ref, out_idx_ref, value_ref, recv_ref, turn_ref,
                   scale_ref, exit_ref, *rest):
    if with_send:
        value_out, send_out, table = rest
    else:
        value_out, table = rest
    blocks = value_ref.shape[0]
    ghosts = out_idx_ref.shape[0]
    slots = col_ref.shape[1]
    block_len = value_ref.shape[1]
    capacity = ghosts // recv_ref.shape[0]
    table[0:blocks] = value_ref[...] * scale_ref[...]
    for p in range(recv_ref.shape[0]):
        table[blocks + p * capacity : blocks + (p + 1) * capacity] = recv_ref[p].T.reshape(
            capacity, block_len, -1
        )
    for n in range(blocks):
        pieces = [table[col_ref[n, s]] * live_factor(cnt_ref, n, s) for s in range(slots)]
        value_out[n] = dot3(turn_ref[n], jnp.concatenate(pieces, axis=0)) + exit_ref[n]
    if with_send:
        for p in range(send_out.shape[0]):
            rows = []
            for c in range(capacity):
                b = out_idx_ref[p * capacity + c]
                rows.append(value_out[b] * scale_ref[b])
            send_out[p] = jnp.concatenate(rows, axis=0).T


def adjoint_kernel(first, cnt_ref, col_ref, out_idx_ref, value_ref, demand_ref, scale_ref,
                   own_ref, returned_ref, turn_ref, extra_ref, own_out, ghost_out, ratio, totals):
    blocks = value_ref.shape[0]
    ghosts = out_idx_ref.shape[0]
    slots = col_ref.shape[1]
    block_len = value_ref.shape[1]
    capacity = ghosts // ghost_out.shape[0]
    if first:
        ratio[...] = demand_ref[...] / value_ref[...]
    else:
        totals[0:blocks] = own_ref[...]
        add_returned(totals, out_idx_ref, returned_ref)
        value = value_ref[...]
        load = value * (totals[0:blocks] * scale_ref[...]) + demand_ref[...]
        ratio[...] = load / value
    totals[...] = jnp.zeros(totals.shape, totals.dtype)
    for n in range(blocks):
        terms = dot3(turn_ref[n], ratio[n])
        for s in range(slots):
            b = col_ref[n, s]
            piece = terms[s * block_len : (s + 1) * block_len, :] * live_factor(cnt_ref, n, s)
            totals[b] = totals[b] + piece
    own_out[...] = totals[0:blocks]
    for p in range(ghost_out.shape[0]):
        part = totals[blocks + p * capacity : blocks + (p + 1) * capacity]
        ghost_out[p, 0 : value_ref.shape[2]] = part.reshape(capacity * block_len, -1).T
        ghost_out[p, value_ref.shape[2] :] = extra_ref[p]


def last_kernel(cnt_ref, col_ref, out_idx_ref, place_ref, value_ref, demand_ref, scale_ref, own_ref,
                returned_ref, turn_ref, weight_ref, routed_out, ratio, totals):
    blocks = value_ref.shape[0]
    ghosts = out_idx_ref.shape[0]
    slots = col_ref.shape[1]
    block_len = value_ref.shape[1]
    columns = value_ref.shape[2]
    capacity = ghosts // returned_ref.shape[0]
    totals[0:blocks] = own_ref[...]
    add_returned(totals, out_idx_ref, returned_ref)
    value = value_ref[...]
    load = value * (totals[0:blocks] * scale_ref[...]) + demand_ref[...]
    ratio[...] = load / value
    totals[...] = jnp.zeros(totals.shape, totals.dtype)
    for n in range(blocks):
        terms = dot3(turn_ref[n], ratio[n])
        for s in range(slots):
            b = col_ref[n, s]
            piece = terms[s * block_len : (s + 1) * block_len, :] * live_factor(cnt_ref, n, s)
            totals[b] = totals[b] + piece
    weight = weight_ref[...]
    routed_out[...] = jnp.zeros(routed_out.shape, routed_out.dtype)
    me = place_ref[0]
    for b in range(blocks):
        product = value_ref[b] * scale_ref[b] * totals[b]
        routed_out[me, b, 0:1, :] = dest_sum(product + demand_ref[b])
        routed_out[me, b, 1:2, :] = dest_sum(weight * product)
    for p in range(returned_ref.shape[0]):
        weighted = returned_ref[p][columns : 2 * columns].T
        for c in range(capacity):
            k = p * capacity + c
            blk = place_ref[1 + k]
            product = weighted[c * block_len : (c + 1) * block_len, :] * totals[blocks + k]
            routed_out[p, blk, 0:1, :] = routed_out[p, blk, 0:1, :] + dest_sum(product)
            routed_out[p, blk, 1:2, :] = routed_out[p, blk, 1:2, :] + dest_sum(weight * product)


def middle_kernel(cnt_ref, col_ref, out_idx_ref, value_ref, recv_ref, turn_ref, scale_ref, exit_ref,
                  demand_ref, turn_t_ref, value_out, own_out, ghost_out, send, table, ratio, totals):
    forward_kernel(True, cnt_ref, col_ref, out_idx_ref, value_ref, recv_ref, turn_ref, scale_ref,
                   exit_ref, value_out, send, table)
    adjoint_kernel(True, cnt_ref, col_ref, out_idx_ref, value_out, demand_ref, scale_ref, demand_ref,
                   demand_ref, turn_t_ref, send, own_out, ghost_out, ratio, totals)


def final_kernel(out_idx_ref, value_ref, demand_ref, scale_ref, own_ref, returned_ref, weight_ref,
                 flow_out, grad_out, owned):
    owned[...] = own_ref[...]
    add_returned(owned, out_idx_ref, returned_ref)
    value = value_ref[...]
    back = owned[...] * scale_ref[...]
    load = value * back + demand_ref[...]
    flow_out[...] = jnp.sum(load, axis=2, keepdims=True)
    grad_out[...] = jnp.sum(weight_ref[...] * value * back, axis=2, keepdims=True)


def local(cost, turn_weight, exit_value, demand, dest_weight, slot_count, col_ref, send_blocks):
    blocks = col_ref.shape[0]
    block_len = turn_weight.shape[1]
    columns = exit_value.shape[0]
    capacity = send_blocks.shape[2]
    partitions = lax.axis_size("dom")
    my_part = lax.axis_index("dom")
    ghosts = partitions * capacity
    own_len = blocks * block_len
    f32 = jnp.float32
    block_shape = (blocks, block_len, columns)
    ghost_shape = (partitions, columns, capacity * block_len)
    turn_t = turn_weight.transpose(0, 2, 1)
    scale = jnp.broadcast_to(jnp.exp(-cost).reshape(blocks, block_len, 1), block_shape)
    outbound = lax.dynamic_index_in_dim(send_blocks, my_part, 0, keepdims=False).reshape(-1)
    smem = pl.BlockSpec(memory_space=pltpu.SMEM)
    vmem = pl.BlockSpec(memory_space=pltpu.VMEM)
    scratch = pltpu.VMEM((blocks + ghosts, block_len, columns), f32)

    def forward(with_send):
        outs = [jax.ShapeDtypeStruct(block_shape, f32)]
        if with_send:
            outs.append(jax.ShapeDtypeStruct(ghost_shape, f32))
        return pl.pallas_call(
            lambda *refs: forward_kernel(with_send, *refs),
            out_shape=tuple(outs),
            in_specs=[smem, smem, smem] + [vmem] * 5,
            out_specs=tuple([vmem] * len(outs)),
            scratch_shapes=[scratch],
        )

    def adjoint(first):
        doubled = (partitions, 2 * columns, capacity * block_len)
        return pl.pallas_call(
            lambda *refs: adjoint_kernel(first, *refs),
            out_shape=(jax.ShapeDtypeStruct(block_shape, f32), jax.ShapeDtypeStruct(doubled, f32)),
            in_specs=[smem, smem, smem] + [vmem] * 7,
            out_specs=(vmem, vmem),
            scratch_shapes=[pltpu.VMEM(block_shape, f32), scratch],
        )

    final = pl.pallas_call(
        final_kernel,
        out_shape=(
            jax.ShapeDtypeStruct((blocks, block_len, 1), f32),
            jax.ShapeDtypeStruct((blocks, block_len, 1), f32),
        ),
        in_specs=[smem] + [vmem] * 6,
        out_specs=(vmem, vmem),
        scratch_shapes=[pltpu.VMEM(block_shape, f32)],
    )

    def exchange(pieces):
        return lax.all_to_all(pieces, "dom", split_axis=0, concat_axis=0, tiled=True)

    exit_t = exit_value.T.reshape(block_shape)
    demand_t = demand.T.reshape(block_shape)
    idx = (slot_count, col_ref, outbound)
    first_send = (exit_value * jnp.exp(-cost)[None, :]).reshape(columns, blocks, block_len)[:, outbound, :]
    received = exchange(
        first_send.reshape(columns, partitions, capacity * block_len).transpose(1, 0, 2)
    )
    value, send = forward(True)(*idx, exit_t, received, turn_weight, scale, exit_t)
    received = exchange(send)
    middle = pl.pallas_call(
        middle_kernel,
        out_shape=(
            jax.ShapeDtypeStruct(block_shape, f32),
            jax.ShapeDtypeStruct(block_shape, f32),
            jax.ShapeDtypeStruct((partitions, 2 * columns, capacity * block_len), f32),
        ),
        in_specs=[smem, smem, smem] + [vmem] * 7,
        out_specs=(vmem, vmem, vmem),
        scratch_shapes=[pltpu.VMEM(ghost_shape, f32), scratch, pltpu.VMEM(block_shape, f32), scratch],
    )
    value, own, ghost = middle(*idx, value, received, turn_weight, scale, exit_t, demand_t, turn_t)
    returned = exchange(ghost)
    weight = dest_weight.reshape(1, columns)
    ghost_part = jnp.arange(ghosts, dtype=jnp.int32) // capacity
    ghost_block = send_blocks[ghost_part, my_part, jnp.arange(ghosts, dtype=jnp.int32) % capacity]
    place = jnp.concatenate([my_part.astype(jnp.int32).reshape(1), ghost_block.astype(jnp.int32)])
    last = pl.pallas_call(
        last_kernel,
        out_shape=jax.ShapeDtypeStruct((partitions, blocks, 2, block_len), f32),
        in_specs=[smem, smem, smem, smem] + [vmem] * 7,
        out_specs=vmem,
        scratch_shapes=[pltpu.VMEM(block_shape, f32), scratch],
    )
    routed = last(*idx, place, value, demand_t, scale, own, returned, turn_t, weight)
    dest_n = lax.axis_size("dest")
    routed = routed.reshape(partitions * dest_n, blocks // dest_n, 2, block_len)
    got = lax.all_to_all(routed, ("dom", "dest"), split_axis=0, concat_axis=0, tiled=True)
    total = jnp.sum(got, axis=0) / (columns * dest_n)
    return (total[:, 0].reshape(-1), -total[:, 1].reshape(-1))


def solution(mesh):
    placed = (
        P("dom"),
        P("dom", None, None),
        P("dest", "dom"),
        P("dest", "dom"),
        P("dest"),
        P("dom"),
        P("dom", None),
        P(),
    )
    return jax.shard_map(
        local,
        mesh=mesh,
        in_specs=placed,
        out_specs=(P(("dom", "dest")), P(("dom", "dest"))),
        check_vma=False,
    )
```
